256 devices in a mesh: dp: 4 (over z_hi, core), ctx: 64 (over x, z_lo, y).
Axes of the slice: x: 4, y: 4, z: 8 (z_hi: 2, z_lo: 4; z = z_hi * 4 + z_lo), core: 2. Of those that a mesh axis runs over, the one named last changes fastest.
Arguments:
- query_rows: bfloat16 [4, 16384, 2048], P('dp', 'ctx'), may hold values from -40 to 40
- key_rows: bfloat16 [4, 16384, 1024], P('dp', 'ctx'), may hold values from -6 to 6
- value_rows: bfloat16 [4, 16384, 1024], P('dp', 'ctx'), may hold values from -6 to 6
- out_grad: bfloat16 [4, 16384, 2048], P('dp', 'ctx'), may hold values from -6 to 6
- gate_grads: bfloat16 [4, 18432, 2304], P('dp', 'ctx'), may hold values from -6 to 6
- first_moment: float32 [18432, 2304], P('ctx', 'dp'), may hold values from -3 to 3
- second_moment: float32 [18432, 2304], P('ctx', 'dp'), may hold values from 0.05 to 2
- master_rows: float32 [18432, 2304], P('ctx', 'dp'), may hold values from -3 to 3
Outputs:
- query_grad: bfloat16 [4, 16384, 2048], P('dp', 'ctx')
- key_grad: bfloat16 [4, 16384, 1024], P('dp', 'ctx')
- value_grad: bfloat16 [4, 16384, 1024], P('dp', 'ctx')
- gate_params: bfloat16 [18432, 2304], P('ctx')
- new_first: float32 [18432, 2304], P('ctx', 'dp')
- new_second: float32 [18432, 2304], P('ctx', 'dp')
- new_master: float32 [18432, 2304], P('ctx', 'dp')
The draws below stay inside these ranges and needn't reach their ends.
All inputs are finite; a program needn't handle non-finite values.
Results may differ from the reference program's by a relative error of at most 0.019.
Values may be sent and summed in bfloat16 or wider, within the bound.
No kernel may reach another device: no remote copies, remote signals or barrier semaphores. Data moves between devices by JAX's collectives and lax.ppermute only.
A program may use at most 192 MiB of HBM per device.

```python
import math
import jax
import jax.numpy as jnp
from jax import lax

HEADS = 16
KV_HEADS = 8
HEAD_DIM = 128
WINDOW = 1024
TOK_DEV = 256
MODEL_DIM = 2304
ADAM_STEP = 10
REPLICAS = 4
LENGTH = 16384
FF = 18432


def shared_keys(key):
    sub = jax.random.fold_in(key, 11)
    shape = (REPLICAS, LENGTH, KV_HEADS, HEAD_DIM)
    keys = jnp.clip(jax.random.normal(sub, shape, jnp.float32), -6.0, 6.0)
    return keys


def draw_key_rows(key, part):
    return shared_keys(key).reshape(REPLICAS, LENGTH, KV_HEADS * HEAD_DIM).astype(jnp.bfloat16)


def draw_query_rows(key, part):
    keys = shared_keys(key)
    group_size = HEADS // KV_HEADS
    shape = (REPLICAS, LENGTH, KV_HEADS, group_size, HEAD_DIM)
    drawn_key = jax.random.fold_in(key, 23)
    drawn = jnp.clip(jax.random.normal(drawn_key, shape, jnp.float32), -6.0, 6.0)
    position = jnp.arange(LENGTH, dtype=jnp.int32)
    reach_top = jnp.minimum(position, WINDOW - 1) + 1
    first_back = jax.random.randint(jax.random.fold_in(key, 31), (REPLICAS, LENGTH), 0, reach_top[None, :])
    second_back = jax.random.randint(jax.random.fold_in(key, 37), (REPLICAS, LENGTH), 0, reach_top[None, :])
    first_index = (position[None, :] - first_back).astype(jnp.int32)
    second_index = (position[None, :] - second_back).astype(jnp.int32)
    marked = jax.random.randint(jax.random.fold_in(key, 41), (REPLICAS, LENGTH), 0, 16) == 0
    first_near = jnp.take_along_axis(keys, first_index[:, :, None, None], axis=1)
    second_near = jnp.take_along_axis(keys, second_index[:, :, None, None], axis=1)
    factor = 12.0 / HEAD_DIM
    high = jax.random.uniform(jax.random.fold_in(key, 43), (REPLICAS, LENGTH, KV_HEADS, group_size, 1), jnp.float32, 30.0, 55.0)
    gap = jax.random.uniform(jax.random.fold_in(key, 47), (REPLICAS, LENGTH, KV_HEADS, group_size, 1), jnp.float32, 1.5, 4.5)
    aligned = high * factor * first_near[:, :, :, None, :] + (high - gap) * factor * second_near[:, :, :, None, :]
    aligned = jnp.clip(aligned, -40.0, 40.0)
    rows = jnp.where(marked[:, :, None, None, None], aligned, drawn)
    return rows.reshape(REPLICAS, LENGTH, HEADS * HEAD_DIM).astype(jnp.bfloat16)


def block_scale(rng, dims, shards, least, top_value):
    factor_of, own = 1.0, jax.random.fold_in(rng, 6)
    for dim, blocks in shards:
        steps = jnp.exp(jax.random.uniform(jax.random.fold_in(own, dim), (blocks,), jnp.float32, least / len(shards), top_value / len(shards)))
        factor_of = factor_of * jnp.repeat(steps, dims[dim] // blocks).reshape([-1 if axis == dim else 1 for axis in range(len(dims))])
    return factor_of


def scatter_about(stream_key, extent, spread, most, shards=(), kind=jnp.bfloat16):
    values = spread * jax.random.normal(stream_key, extent, jnp.float32)
    if shards:
        values = values * block_scale(stream_key, extent, shards, -0.22, 0.18)
    return jnp.clip(values, -most, most).astype(kind)


def setup_inputs(seed: int = 0) -> dict:
    key_list = jax.random.split(jax.random.key(seed), 9)
    query_rows = draw_query_rows(jax.random.fold_in(key_list[8], 71), 0)
    key_rows = draw_key_rows(jax.random.fold_in(key_list[8], 71), 0)
    value_rows = scatter_about(key_list[2], (REPLICAS, LENGTH, KV_HEADS * HEAD_DIM), 1.0, 6.0, ((0, 4), (1, 64)))
    out_grad = scatter_about(key_list[3], (REPLICAS, LENGTH, HEADS * HEAD_DIM), 1.0, 6.0, ((0, 4), (1, 64)))
    gate_grads = scatter_about(key_list[4], (REPLICAS, FF, MODEL_DIM), 1.0, 6.0, ((0, 4), (1, 64)))
    first_moment = scatter_about(key_list[5], (FF, MODEL_DIM), 0.5, 3.0, ((0, 64), (1, 4)), jnp.float32)
    second_moment = jnp.clip(jnp.exp(math.log(2.0) - 3.6888794 * jax.random.uniform(key_list[6], (FF, MODEL_DIM), jnp.float32) ** block_scale(key_list[6], (FF, MODEL_DIM), ((0, 64), (1, 4)), -0.2, 0.2)), 0.05, 2.0)
    master_rows = scatter_about(key_list[7], (FF, MODEL_DIM), 0.5, 3.0, ((0, 64), (1, 4)), jnp.float32)
    return dict(query_rows=query_rows, key_rows=key_rows, value_rows=value_rows, out_grad=out_grad, gate_grads=gate_grads, first_moment=first_moment, second_moment=second_moment, master_rows=master_rows)


SOFT_CAP = 50.0
SCORE_SCALE = 1.0 / 12.0
LEARN_RATE = 0.01
BETA_ONE = 0.9
BETA_TWO = 0.95
EPSILON = 1e-08

def block_grads(query_heads, grad_heads, key_heads, value_heads, visible):
    f32 = jnp.float32
    raw_scores = jnp.einsum('agrd,bgd->grab', query_heads.astype(f32), key_heads.astype(f32)) * SCORE_SCALE
    capped = SOFT_CAP * jnp.tanh(raw_scores / SOFT_CAP)
    weights = jnp.where(visible[None, None], jnp.exp(capped), 0.0).astype(jnp.bfloat16)
    totals = lax.optimization_barrier(jnp.sum(weights.astype(f32), axis=3))
    weighted = jnp.einsum('grab,bgd->agrd', weights.astype(f32), value_heads.astype(f32))
    attended = (weighted / jnp.transpose(totals, (2, 0, 1))[..., None]).astype(jnp.bfloat16)
    deltas = jnp.transpose(lax.optimization_barrier(jnp.sum(grad_heads.astype(f32) * attended.astype(f32), axis=3)), (1, 2, 0))
    normed = weights.astype(f32) / totals[..., None]
    rounded_probs = normed.astype(jnp.bfloat16)
    prob_grad = jnp.einsum('agrd,bgd->grab', grad_heads.astype(f32), value_heads.astype(f32))
    score_grad = (normed * (prob_grad - deltas[..., None]) * (1.0 - (capped / SOFT_CAP) ** 2)).astype(jnp.bfloat16)
    query_grad = (jnp.einsum('grab,bgd->agrd', score_grad.astype(f32), key_heads.astype(f32)) * SCORE_SCALE).astype(jnp.bfloat16)
    key_part = jnp.einsum('grab,agrd->bgd', score_grad.astype(f32), query_heads.astype(f32))
    value_part = jnp.einsum('grab,agrd->bgd', rounded_probs.astype(f32), grad_heads.astype(f32))
    return (query_grad, key_part, value_part)

def one_sequence(inputs):
    query_rows, key_rows, value_rows, out_grad = inputs
    seq_len = query_rows.shape[0]
    group_size = HEADS // KV_HEADS
    block_rows = TOK_DEV
    query_heads = query_rows.reshape(seq_len, KV_HEADS, group_size, HEAD_DIM)
    grad_heads = out_grad.reshape(seq_len, KV_HEADS, group_size, HEAD_DIM)
    zeros_pad = jnp.zeros((WINDOW, KV_HEADS, HEAD_DIM), jnp.bfloat16)
    key_pad = jnp.concatenate([zeros_pad, key_rows.reshape(seq_len, KV_HEADS, HEAD_DIM)], axis=0)
    value_pad = jnp.concatenate([zeros_pad, value_rows.reshape(seq_len, KV_HEADS, HEAD_DIM)], axis=0)

    def step_block(running, block_index):
        key_acc, value_acc = running
        first_row = (block_index * block_rows).astype(jnp.int32)
        query_block = lax.dynamic_slice_in_dim(query_heads, first_row, block_rows, 0)
        grad_block = lax.dynamic_slice_in_dim(grad_heads, first_row, block_rows, 0)
        key_block = lax.dynamic_slice_in_dim(key_pad, first_row, block_rows + WINDOW, 0)
        value_block = lax.dynamic_slice_in_dim(value_pad, first_row, block_rows + WINDOW, 0)
        query_pos = first_row + jnp.arange(block_rows, dtype=jnp.int32)
        key_pos = first_row - WINDOW + jnp.arange(block_rows + WINDOW, dtype=jnp.int32)
        distance = query_pos[:, None] - key_pos[None, :]
        visible = (key_pos[None, :] >= 0) & (distance >= 0) & (distance < WINDOW)
        query_grad, key_part, value_part = block_grads(query_block, grad_block, key_block, value_block, visible)
        key_old = lax.dynamic_slice_in_dim(key_acc, first_row, block_rows + WINDOW, 0)
        value_old = lax.dynamic_slice_in_dim(value_acc, first_row, block_rows + WINDOW, 0)
        key_acc = lax.dynamic_update_slice_in_dim(key_acc, key_old + key_part, first_row, 0)
        value_acc = lax.dynamic_update_slice_in_dim(value_acc, value_old + value_part, first_row, 0)
        return ((key_acc, value_acc), query_grad)
    start_acc = jnp.zeros((seq_len + WINDOW, KV_HEADS, HEAD_DIM), jnp.float32)
    (key_acc, value_acc), query_blocks = lax.scan(step_block, (start_acc, start_acc), jnp.arange(seq_len // block_rows, dtype=jnp.int32))
    query_grad = query_blocks.reshape(seq_len, HEADS * HEAD_DIM)
    key_grad = (key_acc[WINDOW:] * SCORE_SCALE).astype(jnp.bfloat16).reshape(seq_len, KV_HEADS * HEAD_DIM)
    value_grad = value_acc[WINDOW:].astype(jnp.bfloat16).reshape(seq_len, KV_HEADS * HEAD_DIM)
    return (query_grad, key_grad, value_grad)

def reference(query_rows, key_rows, value_rows, out_grad, gate_grads, first_moment, second_moment, master_rows):
    query_grad, key_grad, value_grad = lax.map(one_sequence, (query_rows, key_rows, value_rows, out_grad))
    summed = lax.optimization_barrier(jnp.sum(gate_grads.astype(jnp.float32), axis=0))
    new_first = BETA_ONE * first_moment + (1.0 - BETA_ONE) * summed
    new_second = BETA_TWO * second_moment + (1.0 - BETA_TWO) * summed * summed
    fix_one = 1.0 - BETA_ONE ** ADAM_STEP
    fix_two = 1.0 - BETA_TWO ** ADAM_STEP
    new_master = master_rows - LEARN_RATE * (new_first / fix_one) / (jnp.sqrt(new_second / fix_two) + EPSILON)
    gate_params = new_master.astype(jnp.bfloat16)
    return (query_grad, key_grad, value_grad, gate_params, new_first, new_second, new_master)
```

```python
import jax
import jax.numpy as jnp
from jax import lax
from jax.sharding import PartitionSpec as P

HEADS = 16
KV_HEADS = 8
HEAD_DIM = 128
WINDOW = 1024
ADAM_STEP = 10


SOFT_CAP = 50.0
SCORE_SCALE = 1.0 / 12.0
LEARN_RATE = 0.01
BETA_ONE = 0.9
BETA_TWO = 0.95
EPSILON = 1e-08


def passed_along(block, axis, distance):
    devices = range(lax.axis_size(axis))
    route = [(i - distance, i) for i in devices if i - distance in devices]
    return lax.ppermute(block, axis, route)


def window_mask(query_start, key_start, query_count, key_count, seq_len):
    query_pos = query_start + lax.iota(jnp.int32, query_count)
    key_pos = key_start + lax.iota(jnp.int32, key_count)
    distance = query_pos[:, None] - key_pos[None, :]
    visible = (
        (key_pos[None, :] >= 0)
        & (query_pos[:, None] < seq_len)
        & (distance >= 0)
        & (distance < WINDOW)
    )
    return (visible, query_pos < seq_len)


def capped_weights(query_heads, key_heads, visible):
    raw_scores = (
        jnp.einsum("agrd,bgd->grab", query_heads, key_heads, preferred_element_type=jnp.float32)
        * SCORE_SCALE
    )
    capped = SOFT_CAP * jnp.tanh(raw_scores / SOFT_CAP)
    weights = jnp.where(visible[None, None], jnp.exp(capped), 0.0).astype(jnp.bfloat16)
    return (capped, weights)


def score_terms(grad_heads, value_heads, capped, weights, totals, deltas):
    normed = weights.astype(jnp.float32) / totals[..., None]
    prob_grad = jnp.einsum(
        "agrd,bgd->grab", grad_heads, value_heads, preferred_element_type=jnp.float32
    )
    score_grad = (
        normed * (prob_grad - deltas[..., None]) * (1.0 - (capped / SOFT_CAP) ** 2)
    ).astype(jnp.bfloat16)
    return (normed.astype(jnp.bfloat16), score_grad)


def on_device(
    query_rows, key_rows, value_rows, out_grad, gate_grads, first_moment, second_moment, master_rows
):
    tokens = query_rows.shape[1]
    group_size = HEADS // KV_HEADS
    ctx_count = lax.axis_size("ctx")
    ctx_index = lax.axis_index("ctx")
    reach = (WINDOW - 1) // tokens + 1
    seq_len = tokens * ctx_count
    query_heads = query_rows[0].reshape(tokens, KV_HEADS, group_size, HEAD_DIM)
    grad_heads = out_grad[0].reshape(tokens, KV_HEADS, group_size, HEAD_DIM)
    key_heads = key_rows[0].reshape(tokens, KV_HEADS, HEAD_DIM)
    value_heads = value_rows[0].reshape(tokens, KV_HEADS, HEAD_DIM)
    packed = jnp.concatenate([key_heads, value_heads], axis=2)
    key_list = []
    value_list = []
    for offset in range(reach, 0, -1):
        shifted = passed_along(packed, "ctx", offset)
        key_list.append(shifted[:, :, :HEAD_DIM])
        value_list.append(shifted[:, :, HEAD_DIM:])
    key_all = jnp.concatenate(key_list + [key_heads], axis=0)
    value_all = jnp.concatenate(value_list + [value_heads], axis=0)
    visible, query_live = window_mask(
        ctx_index * tokens, (ctx_index - reach) * tokens, tokens, (reach + 1) * tokens, seq_len
    )
    capped, weights = capped_weights(query_heads, key_all, visible)
    totals = jnp.sum(weights.astype(jnp.float32), axis=3)
    weighted = jnp.einsum("grab,bgd->agrd", weights, value_all, preferred_element_type=jnp.float32)
    attended = (weighted / jnp.transpose(totals, (2, 0, 1))[..., None]).astype(jnp.bfloat16)
    deltas = jnp.transpose(
        jnp.sum(grad_heads.astype(jnp.float32) * attended.astype(jnp.float32), axis=3), (1, 2, 0)
    )
    rounded, score_grad = score_terms(grad_heads, value_all, capped, weights, totals, deltas)
    query_grad = (
        jnp.einsum("grab,bgd->agrd", score_grad, key_all, preferred_element_type=jnp.float32)
        * SCORE_SCALE
    ).astype(jnp.bfloat16)
    key_part = jnp.einsum(
        "grab,agrd->bgd", score_grad, query_heads, preferred_element_type=jnp.float32
    )
    value_part = jnp.einsum(
        "grab,agrd->bgd", rounded, grad_heads, preferred_element_type=jnp.float32
    )
    key_acc = key_part[reach * tokens :]
    value_acc = value_part[reach * tokens :]
    for offset in range(1, reach + 1):
        first_row = (reach - offset) * tokens
        outgoing = jnp.concatenate(
            [key_part[first_row : first_row + tokens], value_part[first_row : first_row + tokens]],
            axis=2,
        ).astype(jnp.bfloat16)
        returned = passed_along(outgoing, "ctx", -offset).astype(jnp.float32)
        key_acc = key_acc + returned[:, :, :HEAD_DIM]
        value_acc = value_acc + returned[:, :, HEAD_DIM:]
    query_out = query_grad.reshape(1, tokens, HEADS * HEAD_DIM)
    key_out = (key_acc * SCORE_SCALE).astype(jnp.bfloat16).reshape(1, tokens, KV_HEADS * HEAD_DIM)
    value_out = value_acc.astype(jnp.bfloat16).reshape(1, tokens, KV_HEADS * HEAD_DIM)
    partial_value = gate_grads[0].astype(jnp.float32)
    summed = lax.psum_scatter(
        partial_value.astype(jnp.bfloat16), "dp", scatter_dimension=1, tiled=True
    ).astype(jnp.float32)
    new_first = BETA_ONE * first_moment + (1.0 - BETA_ONE) * summed
    new_second = BETA_TWO * second_moment + (1.0 - BETA_TWO) * summed * summed
    fix_one = 1.0 - BETA_ONE**ADAM_STEP
    fix_two = 1.0 - BETA_TWO**ADAM_STEP
    new_master = master_rows - LEARN_RATE * (new_first / fix_one) / (
        jnp.sqrt(new_second / fix_two) + EPSILON
    )
    gate_params = lax.all_gather(new_master.astype(jnp.bfloat16), "dp", axis=1, tiled=True)
    return (query_out, key_out, value_out, gate_params, new_first, new_second, new_master)


def solution(mesh):
    placed = (
        P("dp", "ctx", None),
        P("dp", "ctx", None),
        P("dp", "ctx", None),
        P("dp", "ctx", None),
        P("dp", "ctx", None),
        P("ctx", "dp"),
        P("ctx", "dp"),
        P("ctx", "dp"),
    )
    return jax.shard_map(
        on_device,
        mesh=mesh,
        in_specs=placed,
        out_specs=(
            P("dp", "ctx", None),
            P("dp", "ctx", None),
            P("dp", "ctx", None),
            P("ctx", None),
            P("ctx", "dp"),
            P("ctx", "dp"),
            P("ctx", "dp"),
        ),
        check_vma=False,
    )
```

```python
import jax
import jax.numpy as jnp
from jax import lax
from jax.sharding import PartitionSpec as P

HEADS = 16
KV_HEADS = 8
HEAD_DIM = 128
WINDOW = 1024
ADAM_STEP = 10


SOFT_CAP = 50.0
SCORE_SCALE = 1.0 / 12.0
LEARN_RATE = 0.01
BETA_ONE = 0.9
BETA_TWO = 0.95
EPSILON = 1e-08


def passed_along(block, axis, distance):
    devices = range(lax.axis_size(axis))
    route = [(i - distance, i) for i in devices if i - distance in devices]
    return lax.ppermute(block, axis, route)


def window_mask(query_start, key_start, query_count, key_count, seq_len):
    query_pos = query_start + lax.iota(jnp.int32, query_count)
    key_pos = key_start + lax.iota(jnp.int32, key_count)
    distance = query_pos[:, None] - key_pos[None, :]
    visible = (
        (key_pos[None, :] >= 0)
        & (query_pos[:, None] < seq_len)
        & (distance >= 0)
        & (distance < WINDOW)
    )
    return (visible, query_pos < seq_len)


def capped_weights(query_heads, key_heads, visible):
    raw_scores = (
        jnp.einsum("agrd,bgd->grab", query_heads, key_heads, preferred_element_type=jnp.float32)
        * SCORE_SCALE
    )
    capped = SOFT_CAP * jnp.tanh(raw_scores / SOFT_CAP)
    weights = jnp.where(visible[None, None], jnp.exp(capped), 0.0).astype(jnp.bfloat16)
    return (capped, weights)


def score_terms(grad_heads, value_heads, capped, weights, totals, deltas):
    normed = weights.astype(jnp.float32) / totals[..., None]
    prob_grad = jnp.einsum(
        "agrd,bgd->grab", grad_heads, value_heads, preferred_element_type=jnp.float32
    )
    score_grad = (
        normed * (prob_grad - deltas[..., None]) * (1.0 - (capped / SOFT_CAP) ** 2)
    ).astype(jnp.bfloat16)
    return (normed.astype(jnp.bfloat16), score_grad)


def chunk_mask(query_start, key_start, tokens):
    query_pos = query_start + lax.iota(jnp.int32, tokens)
    key_pos = key_start + lax.iota(jnp.int32, tokens)
    distance = query_pos[:, None] - key_pos[None, :]
    return (key_pos[None, :] >= 0) & (distance >= 0) & (distance < WINDOW)


def on_device(
    query_rows, key_rows, value_rows, out_grad, gate_grads, first_moment, second_moment, master_rows
):
    tokens = query_rows.shape[1]
    group_size = HEADS // KV_HEADS
    ctx_index = lax.axis_index("ctx")
    reach = (WINDOW - 1) // tokens + 1
    query_heads = query_rows[0].reshape(tokens, KV_HEADS, group_size, HEAD_DIM)
    grad_heads = out_grad[0].reshape(tokens, KV_HEADS, group_size, HEAD_DIM)
    key_heads = key_rows[0].reshape(tokens, KV_HEADS, HEAD_DIM)
    value_heads = value_rows[0].reshape(tokens, KV_HEADS, HEAD_DIM)
    packed = jnp.concatenate([key_heads, value_heads], axis=2)
    chunk_keys = {0: key_heads}
    chunk_values = {0: value_heads}
    for offset in range(1, reach + 1):
        shifted = passed_along(packed, "ctx", offset)
        chunk_keys[offset] = shifted[:, :, :HEAD_DIM]
        chunk_values[offset] = shifted[:, :, HEAD_DIM:]
    query_start = ctx_index * tokens
    capped = {}
    weights = {}
    totals = None
    weighted = None
    for c in range(reach + 1):
        visible = chunk_mask(query_start, (ctx_index - c) * tokens, tokens)
        capped[c], weights[c] = capped_weights(query_heads, chunk_keys[c], visible)
        part_total = jnp.sum(weights[c].astype(jnp.float32), axis=3)
        part_weighted = jnp.einsum(
            "grab,bgd->agrd", weights[c], chunk_values[c], preferred_element_type=jnp.float32
        )
        totals = part_total if totals is None else totals + part_total
        weighted = part_weighted if weighted is None else weighted + part_weighted
    attended = (weighted / jnp.transpose(totals, (2, 0, 1))[..., None]).astype(jnp.bfloat16)
    deltas = jnp.transpose(
        jnp.sum(grad_heads.astype(jnp.float32) * attended.astype(jnp.float32), axis=3), (1, 2, 0)
    )
    query_acc = None
    key_acc = None
    value_acc = None
    for c in range(reach, -1, -1):
        rounded, score_grad = score_terms(
            grad_heads, chunk_values[c], capped[c], weights[c], totals, deltas
        )
        part_query = jnp.einsum(
            "grab,bgd->agrd", score_grad, chunk_keys[c], preferred_element_type=jnp.float32
        )
        query_acc = part_query if query_acc is None else query_acc + part_query
        key_part = jnp.einsum(
            "grab,agrd->bgd", score_grad, query_heads, preferred_element_type=jnp.float32
        )
        value_part = jnp.einsum(
            "grab,agrd->bgd", rounded, grad_heads, preferred_element_type=jnp.float32
        )
        if c == 0:
            own_key, own_value = key_part, value_part
            continue
        outgoing = jnp.concatenate([key_part, value_part], axis=2).astype(jnp.bfloat16)
        returned = passed_along(outgoing, "ctx", -c).astype(jnp.float32)
        key_acc = returned[:, :, :HEAD_DIM] if key_acc is None else key_acc + returned[:, :, :HEAD_DIM]
        value_acc = (
            returned[:, :, HEAD_DIM:] if value_acc is None else value_acc + returned[:, :, HEAD_DIM:]
        )
    key_acc = own_key + key_acc
    value_acc = own_value + value_acc
    query_grad = (query_acc * SCORE_SCALE).astype(jnp.bfloat16)
    query_out = query_grad.reshape(1, tokens, HEADS * HEAD_DIM)
    key_out = (key_acc * SCORE_SCALE).astype(jnp.bfloat16).reshape(1, tokens, KV_HEADS * HEAD_DIM)
    value_out = value_acc.astype(jnp.bfloat16).reshape(1, tokens, KV_HEADS * HEAD_DIM)
    partial_value = gate_grads[0].astype(jnp.float32)
    summed = lax.psum_scatter(
        partial_value.astype(jnp.bfloat16), "dp", scatter_dimension=1, tiled=True
    ).astype(jnp.float32)
    new_first = BETA_ONE * first_moment + (1.0 - BETA_ONE) * summed
    new_second = BETA_TWO * second_moment + (1.0 - BETA_TWO) * summed * summed
    fix_one = 1.0 - BETA_ONE**ADAM_STEP
    fix_two = 1.0 - BETA_TWO**ADAM_STEP
    new_master = master_rows - LEARN_RATE * (new_first / fix_one) / (
        jnp.sqrt(new_second / fix_two) + EPSILON
    )
    gate_params = lax.all_gather(new_master.astype(jnp.bfloat16), "dp", axis=1, tiled=True)
    return (query_out, key_out, value_out, gate_params, new_first, new_second, new_master)


def solution(mesh):
    placed = (
        P("dp", "ctx", None),
        P("dp", "ctx", None),
        P("dp", "ctx", None),
        P("dp", "ctx", None),
        P("dp", "ctx", None),
        P("ctx", "dp"),
        P("ctx", "dp"),
        P("ctx", "dp"),
    )
    return jax.shard_map(
        on_device,
        mesh=mesh,
        in_specs=placed,
        out_specs=(
            P("dp", "ctx", None),
            P("dp", "ctx", None),
            P("dp", "ctx", None),
            P("ctx", None),
            P("ctx", "dp"),
            P("ctx", "dp"),
            P("ctx", "dp"),
        ),
        check_vma=False,
    )
```

```python
import jax
import jax.numpy as jnp
from jax import lax
from jax.sharding import PartitionSpec as P

HEADS = 16
KV_HEADS = 8
HEAD_DIM = 128
WINDOW = 1024
ADAM_STEP = 10


SOFT_CAP = 50.0
SCORE_SCALE = 1.0 / 12.0
LEARN_RATE = 0.01
BETA_ONE = 0.9
BETA_TWO = 0.95
EPSILON = 1e-08


def passed_along(block, axis, distance):
    devices = range(lax.axis_size(axis))
    route = [(i - distance, i) for i in devices if i - distance in devices]
    return lax.ppermute(block, axis, route)


RING = 4


def ring_send(block, delta, senders):
    count = lax.axis_size("ctx")
    route = []
    for c in range(count):
        y = c % RING
        if y in senders:
            route.append((c, c - y + (y + delta) % RING))
    return lax.ppermute(block, "ctx", route)


def window_mask(query_start, key_start, query_count, key_count, seq_len):
    query_pos = query_start + lax.iota(jnp.int32, query_count)
    key_pos = key_start + lax.iota(jnp.int32, key_count)
    distance = query_pos[:, None] - key_pos[None, :]
    visible = (
        (key_pos[None, :] >= 0)
        & (query_pos[:, None] < seq_len)
        & (distance >= 0)
        & (distance < WINDOW)
    )
    return (visible, query_pos < seq_len)


def capped_weights(query_heads, key_heads, visible):
    raw_scores = (
        jnp.einsum("agrd,bgd->grab", query_heads, key_heads, preferred_element_type=jnp.float32)
        * SCORE_SCALE
    )
    capped = SOFT_CAP * jnp.tanh(raw_scores / SOFT_CAP)
    weights = jnp.where(visible[None, None], jnp.exp(capped), 0.0).astype(jnp.bfloat16)
    return (capped, weights)


def score_terms(grad_heads, value_heads, capped, weights, totals, deltas):
    normed = weights.astype(jnp.float32) / totals[..., None]
    prob_grad = jnp.einsum(
        "agrd,bgd->grab", grad_heads, value_heads, preferred_element_type=jnp.float32
    )
    score_grad = (
        normed * (prob_grad - deltas[..., None]) * (1.0 - (capped / SOFT_CAP) ** 2)
    ).astype(jnp.bfloat16)
    return (normed.astype(jnp.bfloat16), score_grad)


def chunk_mask(query_start, key_start, tokens):
    query_pos = query_start + lax.iota(jnp.int32, tokens)
    key_pos = key_start + lax.iota(jnp.int32, tokens)
    distance = query_pos[:, None] - key_pos[None, :]
    return (key_pos[None, :] >= 0) & (distance >= 0) & (distance < WINDOW)


def on_device(
    query_rows, key_rows, value_rows, out_grad, gate_grads, first_moment, second_moment, master_rows
):
    tokens = query_rows.shape[1]
    group_size = HEADS // KV_HEADS
    ctx_index = lax.axis_index("ctx")
    reach = (WINDOW - 1) // tokens + 1
    query_heads = query_rows[0].reshape(tokens, KV_HEADS, group_size, HEAD_DIM)
    grad_heads = out_grad[0].reshape(tokens, KV_HEADS, group_size, HEAD_DIM)
    key_heads = key_rows[0].reshape(tokens, KV_HEADS, HEAD_DIM)
    value_heads = value_rows[0].reshape(tokens, KV_HEADS, HEAD_DIM)
    assert reach == RING and lax.axis_size("ctx") % RING == 0
    packed = jnp.concatenate([key_heads, value_heads], axis=2)
    half = tokens // 2
    prev = passed_along(packed, "ctx", RING)
    chunk_packed = {0: packed, RING: prev}
    chunk_packed[1] = ring_send(packed, 1, {0, 1, 2}) + ring_send(prev, 1, {3})
    chunk_packed[3] = ring_send(packed, -1, {0}) + ring_send(prev, -1, {1, 2, 3})
    relay_a = ring_send(packed[:half], 1, {0, 1}) + ring_send(prev[:half], 1, {2, 3})
    relay_b = ring_send(packed[half:], -1, {0, 1}) + ring_send(prev[half:], -1, {2, 3})
    chunk_packed[2] = jnp.concatenate(
        [ring_send(relay_a, 1, set(range(RING))), ring_send(relay_b, -1, set(range(RING)))], axis=0
    )
    chunk_keys = {}
    chunk_values = {}
    for c, block in chunk_packed.items():
        chunk_keys[c] = block[:, :, :HEAD_DIM]
        chunk_values[c] = block[:, :, HEAD_DIM:]
    query_start = ctx_index * tokens
    capped = {}
    weights = {}
    totals = None
    weighted = None
    for c in range(reach + 1):
        visible = chunk_mask(query_start, (ctx_index - c) * tokens, tokens)
        capped[c], weights[c] = capped_weights(query_heads, chunk_keys[c], visible)
        part_total = jnp.sum(weights[c].astype(jnp.float32), axis=3)
        part_weighted = jnp.einsum(
            "grab,bgd->agrd", weights[c], chunk_values[c], preferred_element_type=jnp.float32
        )
        totals = part_total if totals is None else totals + part_total
        weighted = part_weighted if weighted is None else weighted + part_weighted
    attended = (weighted / jnp.transpose(totals, (2, 0, 1))[..., None]).astype(jnp.bfloat16)
    deltas = jnp.transpose(
        jnp.sum(grad_heads.astype(jnp.float32) * attended.astype(jnp.float32), axis=3), (1, 2, 0)
    )
    query_acc = None
    parts = {}
    for c in (3, 2, 1, RING, 0):
        rounded, score_grad = score_terms(
            grad_heads, chunk_values[c], capped[c], weights[c], totals, deltas
        )
        part_query = jnp.einsum(
            "grab,bgd->agrd", score_grad, chunk_keys[c], preferred_element_type=jnp.float32
        )
        query_acc = part_query if query_acc is None else query_acc + part_query
        key_part = jnp.einsum(
            "grab,agrd->bgd", score_grad, query_heads, preferred_element_type=jnp.float32
        )
        value_part = jnp.einsum(
            "grab,agrd->bgd", rounded, grad_heads, preferred_element_type=jnp.float32
        )
        parts[c] = jnp.concatenate([key_part, value_part], axis=2)
        if c == 3:
            out3 = parts[3].astype(jnp.bfloat16)
            own_back = [ring_send(out3, 1, {3})]
            prev_back = [ring_send(out3, 1, {0, 1, 2})]
        elif c == 2:
            out2 = parts[2].astype(jnp.bfloat16)
            relay_a = ring_send(out2[:half], -1, set(range(RING)))
            relay_b = ring_send(out2[half:], 1, set(range(RING)))
            own2 = jnp.concatenate(
                [ring_send(relay_a, -1, {1, 2}), ring_send(relay_b, 1, {3, 0})], axis=0
            )
            prev2 = jnp.concatenate(
                [ring_send(relay_a, -1, {3, 0}), ring_send(relay_b, 1, {1, 2})], axis=0
            )
        elif c == 1:
            out1 = parts[1].astype(jnp.bfloat16)
            own_back.append(ring_send(out1, -1, {1, 2, 3}))
            prev_back.append(ring_send(out1, -1, {0}))
    own_back.append(own2)
    prev_back.append(prev2)
    prev_acc = parts[RING]
    for block in prev_back:
        prev_acc = prev_acc + block.astype(jnp.float32)
    own_acc = parts[0]
    for block in own_back:
        own_acc = own_acc + block.astype(jnp.float32)
    own_acc = own_acc + passed_along(prev_acc.astype(jnp.bfloat16), "ctx", -RING).astype(
        jnp.float32
    )
    key_acc = own_acc[:, :, :HEAD_DIM]
    value_acc = own_acc[:, :, HEAD_DIM:]
    query_grad = (query_acc * SCORE_SCALE).astype(jnp.bfloat16)
    query_out = query_grad.reshape(1, tokens, HEADS * HEAD_DIM)
    key_out = (key_acc * SCORE_SCALE).astype(jnp.bfloat16).reshape(1, tokens, KV_HEADS * HEAD_DIM)
    value_out = value_acc.astype(jnp.bfloat16).reshape(1, tokens, KV_HEADS * HEAD_DIM)
    partial_value = gate_grads[0].astype(jnp.float32)
    summed = lax.psum_scatter(
        partial_value.astype(jnp.bfloat16), "dp", scatter_dimension=1, tiled=True
    ).astype(jnp.float32)
    new_first = BETA_ONE * first_moment + (1.0 - BETA_ONE) * summed
    new_second = BETA_TWO * second_moment + (1.0 - BETA_TWO) * summed * summed
    fix_one = 1.0 - BETA_ONE**ADAM_STEP
    fix_two = 1.0 - BETA_TWO**ADAM_STEP
    new_master = master_rows - LEARN_RATE * (new_first / fix_one) / (
        jnp.sqrt(new_second / fix_two) + EPSILON
    )
    gate_params = lax.all_gather(new_master.astype(jnp.bfloat16), "dp", axis=1, tiled=True)
    return (query_out, key_out, value_out, gate_params, new_first, new_second, new_master)


def solution(mesh):
    placed = (
        P("dp", "ctx", None),
        P("dp", "ctx", None),
        P("dp", "ctx", None),
        P("dp", "ctx", None),
        P("dp", "ctx", None),
        P("ctx", "dp"),
        P("ctx", "dp"),
        P("ctx", "dp"),
    )
    return jax.shard_map(
        on_device,
        mesh=mesh,
        in_specs=placed,
        out_specs=(
            P("dp", "ctx", None),
            P("dp", "ctx", None),
            P("dp", "ctx", None),
            P("ctx", None),
            P("ctx", "dp"),
            P("ctx", "dp"),
            P("ctx", "dp"),
        ),
        check_vma=False,
    )
```

```python
import jax
import jax.numpy as jnp
from jax import lax
from jax.sharding import PartitionSpec as P

HEADS = 16
KV_HEADS = 8
HEAD_DIM = 128
WINDOW = 1024
ADAM_STEP = 10


SOFT_CAP = 50.0
SCORE_SCALE = 1.0 / 12.0
LEARN_RATE = 0.01
BETA_ONE = 0.9
BETA_TWO = 0.95
EPSILON = 1e-08


def passed_along(block, axis, distance):
    devices = range(lax.axis_size(axis))
    route = [(i - distance, i) for i in devices if i - distance in devices]
    return lax.ppermute(block, axis, route)


RING = 4


def ring_send(block, delta, senders):
    count = lax.axis_size("ctx")
    route = []
    for c in range(count):
        y = c % RING
        if y in senders:
            route.append((c, c - y + (y + delta) % RING))
    return lax.ppermute(block, "ctx", route)


def window_mask(query_start, key_start, query_count, key_count, seq_len):
    query_pos = query_start + lax.iota(jnp.int32, query_count)
    key_pos = key_start + lax.iota(jnp.int32, key_count)
    distance = query_pos[:, None] - key_pos[None, :]
    visible = (
        (key_pos[None, :] >= 0)
        & (query_pos[:, None] < seq_len)
        & (distance >= 0)
        & (distance < WINDOW)
    )
    return (visible, query_pos < seq_len)


def capped_weights(query_heads, key_heads, visible):
    raw_scores = (
        jnp.einsum("agrd,bgd->grab", query_heads, key_heads, preferred_element_type=jnp.float32)
        * SCORE_SCALE
    )
    capped = SOFT_CAP * jnp.tanh(raw_scores / SOFT_CAP)
    weights = jnp.where(visible[None, None], jnp.exp(capped), 0.0).astype(jnp.bfloat16)
    return (capped, weights)


def score_terms(grad_heads, value_heads, capped, weights, totals, deltas):
    normed = weights.astype(jnp.float32) / totals[..., None]
    prob_grad = jnp.einsum(
        "agrd,bgd->grab", grad_heads, value_heads, preferred_element_type=jnp.float32
    )
    score_grad = (
        normed * (prob_grad - deltas[..., None]) * (1.0 - (capped / SOFT_CAP) ** 2)
    ).astype(jnp.bfloat16)
    return (normed.astype(jnp.bfloat16), score_grad)


def chunk_mask(query_start, key_start, tokens):
    query_pos = query_start + lax.iota(jnp.int32, tokens)
    key_pos = key_start + lax.iota(jnp.int32, tokens)
    distance = query_pos[:, None] - key_pos[None, :]
    return (key_pos[None, :] >= 0) & (distance >= 0) & (distance < WINDOW)


def finish_prev(own_back, prev_back, own2, prev2, parts, capped_own, weights_own):
    own_back.append(own2)
    prev_back.append(prev2)
    prev_acc = parts[RING]
    for block in prev_back:
        prev_acc = prev_acc + block.astype(jnp.float32)
    return lax.optimization_barrier((prev_acc.astype(jnp.bfloat16), capped_own, weights_own))


def on_device(
    query_rows, key_rows, value_rows, out_grad, gate_grads, first_moment, second_moment, master_rows
):
    tokens = query_rows.shape[1]
    group_size = HEADS // KV_HEADS
    ctx_index = lax.axis_index("ctx")
    reach = (WINDOW - 1) // tokens + 1
    query_heads = query_rows[0].reshape(tokens, KV_HEADS, group_size, HEAD_DIM)
    grad_heads = out_grad[0].reshape(tokens, KV_HEADS, group_size, HEAD_DIM)
    key_heads = key_rows[0].reshape(tokens, KV_HEADS, HEAD_DIM)
    value_heads = value_rows[0].reshape(tokens, KV_HEADS, HEAD_DIM)
    assert reach == RING and lax.axis_size("ctx") % RING == 0
    packed = jnp.concatenate([key_heads, value_heads], axis=2)
    half = tokens // 2
    prev = passed_along(packed, "ctx", RING)
    chunk_packed = {0: packed, RING: prev}
    chunk_packed[1] = ring_send(packed, 1, {0, 1, 2}) + ring_send(prev, 1, {3})
    chunk_packed[3] = ring_send(packed, -1, {0}) + ring_send(prev, -1, {1, 2, 3})
    relay_a = ring_send(packed[:half], 1, {0, 1}) + ring_send(prev[:half], 1, {2, 3})
    relay_b = ring_send(packed[half:], -1, {0, 1}) + ring_send(prev[half:], -1, {2, 3})
    chunk_packed[2] = jnp.concatenate(
        [ring_send(relay_a, 1, set(range(RING))), ring_send(relay_b, -1, set(range(RING)))], axis=0
    )
    chunk_keys = {}
    chunk_values = {}
    for c, block in chunk_packed.items():
        chunk_keys[c] = block[:, :, :HEAD_DIM]
        chunk_values[c] = block[:, :, HEAD_DIM:]
    query_start = ctx_index * tokens
    capped = {}
    weights = {}
    totals = None
    weighted = None
    for c in range(reach + 1):
        visible = chunk_mask(query_start, (ctx_index - c) * tokens, tokens)
        capped[c], weights[c] = capped_weights(query_heads, chunk_keys[c], visible)
        part_total = jnp.sum(weights[c].astype(jnp.float32), axis=3)
        part_weighted = jnp.einsum(
            "grab,bgd->agrd", weights[c], chunk_values[c], preferred_element_type=jnp.float32
        )
        totals = part_total if totals is None else totals + part_total
        weighted = part_weighted if weighted is None else weighted + part_weighted
    attended = (weighted / jnp.transpose(totals, (2, 0, 1))[..., None]).astype(jnp.bfloat16)
    deltas = jnp.transpose(
        jnp.sum(grad_heads.astype(jnp.float32) * attended.astype(jnp.float32), axis=3), (1, 2, 0)
    )
    partial_value = gate_grads[0].astype(jnp.float32)
    summed = lax.psum_scatter(
        partial_value.astype(jnp.bfloat16), "dp", scatter_dimension=1, tiled=True
    ).astype(jnp.float32)
    new_first = BETA_ONE * first_moment + (1.0 - BETA_ONE) * summed
    new_second = BETA_TWO * second_moment + (1.0 - BETA_TWO) * summed * summed
    fix_one = 1.0 - BETA_ONE**ADAM_STEP
    fix_two = 1.0 - BETA_TWO**ADAM_STEP
    new_master = master_rows - LEARN_RATE * (new_first / fix_one) / (
        jnp.sqrt(new_second / fix_two) + EPSILON
    )
    gate_bf16, deltas = lax.optimization_barrier((new_master.astype(jnp.bfloat16), deltas))
    query_acc = None
    parts = {}
    for c in (3, 2, 1, RING, 0):
        if c == 0:
            prev_out, capped[0], weights[0] = finish_prev(own_back, prev_back, own2, prev2, parts, capped[0], weights[0])
        rounded, score_grad = score_terms(
            grad_heads, chunk_values[c], capped[c], weights[c], totals, deltas
        )
        part_query = jnp.einsum(
            "grab,bgd->agrd", score_grad, chunk_keys[c], preferred_element_type=jnp.float32
        )
        query_acc = part_query if query_acc is None else query_acc + part_query
        key_part = jnp.einsum(
            "grab,agrd->bgd", score_grad, query_heads, preferred_element_type=jnp.float32
        )
        value_part = jnp.einsum(
            "grab,agrd->bgd", rounded, grad_heads, preferred_element_type=jnp.float32
        )
        parts[c] = jnp.concatenate([key_part, value_part], axis=2)
        if c == 3:
            out3 = parts[3].astype(jnp.bfloat16)
            own_back = [ring_send(out3, 1, {3})]
            prev_back = [ring_send(out3, 1, {0, 1, 2})]
        elif c == 2:
            out2 = parts[2].astype(jnp.bfloat16)
            relay_a = ring_send(out2[:half], -1, set(range(RING)))
            relay_b = ring_send(out2[half:], 1, set(range(RING)))
            own2 = jnp.concatenate(
                [ring_send(relay_a, -1, {1, 2}), ring_send(relay_b, 1, {3, 0})], axis=0
            )
            prev2 = jnp.concatenate(
                [ring_send(relay_a, -1, {3, 0}), ring_send(relay_b, 1, {1, 2})], axis=0
            )
        elif c == 1:
            out1 = parts[1].astype(jnp.bfloat16)
            own_back.append(ring_send(out1, -1, {1, 2, 3}))
            prev_back.append(ring_send(out1, -1, {0}))
    own_acc = parts[0]
    for block in own_back:
        own_acc = own_acc + block.astype(jnp.float32)
    own_acc = own_acc + passed_along(prev_out, "ctx", -RING).astype(jnp.float32)
    key_acc = own_acc[:, :, :HEAD_DIM]
    value_acc = own_acc[:, :, HEAD_DIM:]
    query_grad = (query_acc * SCORE_SCALE).astype(jnp.bfloat16)
    query_out = query_grad.reshape(1, tokens, HEADS * HEAD_DIM)
    key_out = (key_acc * SCORE_SCALE).astype(jnp.bfloat16).reshape(1, tokens, KV_HEADS * HEAD_DIM)
    value_out = value_acc.astype(jnp.bfloat16).reshape(1, tokens, KV_HEADS * HEAD_DIM)
    gate_params = lax.all_gather(gate_bf16, "dp", axis=1, tiled=True)
    return (query_out, key_out, value_out, gate_params, new_first, new_second, new_master)


def solution(mesh):
    placed = (
        P("dp", "ctx", None),
        P("dp", "ctx", None),
        P("dp", "ctx", None),
        P("dp", "ctx", None),
        P("dp", "ctx", None),
        P("ctx", "dp"),
        P("ctx", "dp"),
        P("ctx", "dp"),
    )
    return jax.shard_map(
        on_device,
        mesh=mesh,
        in_specs=placed,
        out_specs=(
            P("dp", "ctx", None),
            P("dp", "ctx", None),
            P("dp", "ctx", None),
            P("ctx", None),
            P("ctx", "dp"),
            P("ctx", "dp"),
            P("ctx", "dp"),
        ),
        check_vma=False,
    )
```

```python
import jax
import jax.numpy as jnp
from jax import lax
from jax.sharding import PartitionSpec as P

HEADS = 16
KV_HEADS = 8
HEAD_DIM = 128
WINDOW = 1024
ADAM_STEP = 10


SOFT_CAP = 50.0
SCORE_SCALE = 1.0 / 12.0
LEARN_RATE = 0.01
BETA_ONE = 0.9
BETA_TWO = 0.95
EPSILON = 1e-08


def passed_along(block, axis, distance):
    devices = range(lax.axis_size(axis))
    route = [(i - distance, i) for i in devices if i - distance in devices]
    return lax.ppermute(block, axis, route)


RING = 4


def ring_send(block, delta, senders):
    count = lax.axis_size("ctx")
    route = []
    for c in range(count):
        y = c % RING
        if y in senders:
            route.append((c, c - y + (y + delta) % RING))
    return lax.ppermute(block, "ctx", route)


def window_mask(query_start, key_start, query_count, key_count, seq_len):
    query_pos = query_start + lax.iota(jnp.int32, query_count)
    key_pos = key_start + lax.iota(jnp.int32, key_count)
    distance = query_pos[:, None] - key_pos[None, :]
    visible = (
        (key_pos[None, :] >= 0)
        & (query_pos[:, None] < seq_len)
        & (distance >= 0)
        & (distance < WINDOW)
    )
    return (visible, query_pos < seq_len)


def capped_weights(query_heads, key_heads, visible):
    raw_scores = (
        jnp.einsum("agrd,bgd->grab", query_heads, key_heads, preferred_element_type=jnp.float32)
        * SCORE_SCALE
    )
    capped = SOFT_CAP * jnp.tanh(raw_scores / SOFT_CAP)
    weights = jnp.where(visible[None, None], jnp.exp(capped), 0.0).astype(jnp.bfloat16)
    return (capped, weights)


def score_terms(grad_heads, value_heads, capped, weights, totals, deltas):
    normed = weights.astype(jnp.float32) / totals[..., None]
    prob_grad = jnp.einsum(
        "agrd,bgd->grab", grad_heads, value_heads, preferred_element_type=jnp.float32
    )
    score_grad = (
        normed * (prob_grad - deltas[..., None]) * (1.0 - (capped / SOFT_CAP) ** 2)
    ).astype(jnp.bfloat16)
    return (normed.astype(jnp.bfloat16), score_grad)


def chunk_mask(query_start, key_start, tokens):
    query_pos = query_start + lax.iota(jnp.int32, tokens)
    key_pos = key_start + lax.iota(jnp.int32, tokens)
    distance = query_pos[:, None] - key_pos[None, :]
    return (key_pos[None, :] >= 0) & (distance >= 0) & (distance < WINDOW)


def picked(condition, block):
    return jnp.where(condition, block.astype(jnp.float32), 0.0)


def on_device(
    query_rows, key_rows, value_rows, out_grad, gate_grads, first_moment, second_moment, master_rows
):
    tokens = query_rows.shape[1]
    group_size = HEADS // KV_HEADS
    ctx_index = lax.axis_index("ctx")
    reach = (WINDOW - 1) // tokens + 1
    query_heads = query_rows[0].reshape(tokens, KV_HEADS, group_size, HEAD_DIM)
    grad_heads = out_grad[0].reshape(tokens, KV_HEADS, group_size, HEAD_DIM)
    key_heads = key_rows[0].reshape(tokens, KV_HEADS, HEAD_DIM)
    value_heads = value_rows[0].reshape(tokens, KV_HEADS, HEAD_DIM)
    assert reach == RING and lax.axis_size("ctx") % RING == 0
    packed = jnp.concatenate([key_heads, value_heads], axis=2)
    half = tokens // 2
    prev = passed_along(packed, "ctx", RING)
    chunk_packed = {0: packed, RING: prev}
    chunk_packed[1] = ring_send(packed, 1, {0, 1, 2}) + ring_send(prev, 1, {3})
    chunk_packed[3] = ring_send(packed, -1, {0}) + ring_send(prev, -1, {1, 2, 3})
    relay_a = ring_send(packed[:half], 1, {0, 1}) + ring_send(prev[:half], 1, {2, 3})
    relay_b = ring_send(packed[half:], -1, {0, 1}) + ring_send(prev[half:], -1, {2, 3})
    chunk_packed[2] = jnp.concatenate(
        [ring_send(relay_a, 1, set(range(RING))), ring_send(relay_b, -1, set(range(RING)))], axis=0
    )
    chunk_keys = {}
    chunk_values = {}
    for c, block in chunk_packed.items():
        chunk_keys[c] = block[:, :, :HEAD_DIM]
        chunk_values[c] = block[:, :, HEAD_DIM:]
    query_start = ctx_index * tokens
    capped = {}
    weights = {}
    totals = None
    weighted = None
    for c in range(reach + 1):
        visible = chunk_mask(query_start, (ctx_index - c) * tokens, tokens)
        capped[c], weights[c] = capped_weights(query_heads, chunk_keys[c], visible)
        part_total = jnp.sum(weights[c].astype(jnp.float32), axis=3)
        part_weighted = jnp.einsum(
            "grab,bgd->agrd", weights[c], chunk_values[c], preferred_element_type=jnp.float32
        )
        totals = part_total if totals is None else totals + part_total
        weighted = part_weighted if weighted is None else weighted + part_weighted
    attended = (weighted / jnp.transpose(totals, (2, 0, 1))[..., None]).astype(jnp.bfloat16)
    deltas = jnp.transpose(
        jnp.sum(grad_heads.astype(jnp.float32) * attended.astype(jnp.float32), axis=3), (1, 2, 0)
    )
    partial_value = gate_grads[0].astype(jnp.float32)
    summed = lax.psum_scatter(
        partial_value.astype(jnp.bfloat16), "dp", scatter_dimension=1, tiled=True
    ).astype(jnp.float32)
    new_first = BETA_ONE * first_moment + (1.0 - BETA_ONE) * summed
    new_second = BETA_TWO * second_moment + (1.0 - BETA_TWO) * summed * summed
    fix_one = 1.0 - BETA_ONE**ADAM_STEP
    fix_two = 1.0 - BETA_TWO**ADAM_STEP
    new_master = master_rows - LEARN_RATE * (new_first / fix_one) / (
        jnp.sqrt(new_second / fix_two) + EPSILON
    )
    gate_bf16, deltas = lax.optimization_barrier((new_master.astype(jnp.bfloat16), deltas))
    query_acc = None
    parts = {}
    ring_pos = ctx_index % RING
    everyone = set(range(RING))
    for c in (3, 2, 1, RING, 0):
        if c == 0:
            returned_1 = going_down[:tokens]
            returned_2 = jnp.concatenate([relay_a, relay_b], axis=0)
            returned_3 = going_up[:tokens]
            prev_in = (
                picked(ring_pos != 0, returned_3)
                + picked(ring_pos == RING - 1, returned_1)
                + picked(ring_pos >= 2, returned_2)
            )
            own_in = (
                picked(ring_pos == 0, returned_3)
                + picked(ring_pos <= RING - 2, returned_1)
                + picked(ring_pos <= 1, returned_2)
            )
            prev_out, capped[0], weights[0] = lax.optimization_barrier(
                ((parts[RING] + prev_in).astype(jnp.bfloat16), capped[0], weights[0])
            )
        rounded, score_grad = score_terms(
            grad_heads, chunk_values[c], capped[c], weights[c], totals, deltas
        )
        part_query = jnp.einsum(
            "grab,bgd->agrd", score_grad, chunk_keys[c], preferred_element_type=jnp.float32
        )
        query_acc = part_query if query_acc is None else query_acc + part_query
        key_part = jnp.einsum(
            "grab,agrd->bgd", score_grad, query_heads, preferred_element_type=jnp.float32
        )
        value_part = jnp.einsum(
            "grab,agrd->bgd", rounded, grad_heads, preferred_element_type=jnp.float32
        )
        parts[c] = jnp.concatenate([key_part, value_part], axis=2)
        if c == 2:
            out3 = parts[3].astype(jnp.bfloat16)
            out2 = parts[2].astype(jnp.bfloat16)
            going_up = ring_send(jnp.concatenate([out3, out2[half:]], axis=0), 1, everyone)
        elif c == 1:
            out1 = parts[1].astype(jnp.bfloat16)
            going_down = ring_send(jnp.concatenate([out1, out2[:half]], axis=0), -1, everyone)
            relay_b = ring_send(going_up[tokens:], 1, everyone)
            relay_a = ring_send(going_down[tokens:], -1, everyone)
    own_acc = parts[0] + own_in
    own_acc = own_acc + passed_along(prev_out, "ctx", -RING).astype(jnp.float32)
    key_acc = own_acc[:, :, :HEAD_DIM]
    value_acc = own_acc[:, :, HEAD_DIM:]
    query_grad = (query_acc * SCORE_SCALE).astype(jnp.bfloat16)
    query_out = query_grad.reshape(1, tokens, HEADS * HEAD_DIM)
    key_out = (key_acc * SCORE_SCALE).astype(jnp.bfloat16).reshape(1, tokens, KV_HEADS * HEAD_DIM)
    value_out = value_acc.astype(jnp.bfloat16).reshape(1, tokens, KV_HEADS * HEAD_DIM)
    gate_params = lax.all_gather(gate_bf16, "dp", axis=1, tiled=True)
    return (query_out, key_out, value_out, gate_params, new_first, new_second, new_master)


def solution(mesh):
    placed = (
        P("dp", "ctx", None),
        P("dp", "ctx", None),
        P("dp", "ctx", None),
        P("dp", "ctx", None),
        P("dp", "ctx", None),
        P("ctx", "dp"),
        P("ctx", "dp"),
        P("ctx", "dp"),
    )
    return jax.shard_map(
        on_device,
        mesh=mesh,
        in_specs=placed,
        out_specs=(
            P("dp", "ctx", None),
            P("dp", "ctx", None),
            P("dp", "ctx", None),
            P("ctx", None),
            P("ctx", "dp"),
            P("ctx", "dp"),
            P("ctx", "dp"),
        ),
        check_vma=False,
    )
```

```python
import jax
import jax.numpy as jnp
from jax import lax
from jax.sharding import PartitionSpec as P

HEADS = 16
KV_HEADS = 8
HEAD_DIM = 128
WINDOW = 1024
ADAM_STEP = 10


SOFT_CAP = 50.0
SCORE_SCALE = 1.0 / 12.0
LEARN_RATE = 0.01
BETA_ONE = 0.9
BETA_TWO = 0.95
EPSILON = 1e-08


def passed_along(block, axis, distance):
    devices = range(lax.axis_size(axis))
    route = [(i - distance, i) for i in devices if i - distance in devices]
    return lax.ppermute(block, axis, route)


RING = 4


def ring_send(block, delta, senders):
    count = lax.axis_size("ctx")
    route = []
    for c in range(count):
        y = c % RING
        if y in senders:
            route.append((c, c - y + (y + delta) % RING))
    return lax.ppermute(block, "ctx", route)


def window_mask(query_start, key_start, query_count, key_count, seq_len):
    query_pos = query_start + lax.iota(jnp.int32, query_count)
    key_pos = key_start + lax.iota(jnp.int32, key_count)
    distance = query_pos[:, None] - key_pos[None, :]
    visible = (
        (key_pos[None, :] >= 0)
        & (query_pos[:, None] < seq_len)
        & (distance >= 0)
        & (distance < WINDOW)
    )
    return (visible, query_pos < seq_len)


def capped_weights(query_heads, key_heads, visible):
    raw_scores = (
        jnp.einsum("agrd,bgd->grab", query_heads, key_heads, preferred_element_type=jnp.float32)
        * SCORE_SCALE
    )
    capped = SOFT_CAP * jnp.tanh(raw_scores / SOFT_CAP)
    weights = jnp.where(visible[None, None], jnp.exp(capped), 0.0).astype(jnp.bfloat16)
    return (capped, weights)


def score_terms(grad_heads, value_heads, capped, weights, totals, deltas):
    normed = weights.astype(jnp.float32) / totals[..., None]
    prob_grad = jnp.einsum(
        "agrd,bgd->grab", grad_heads, value_heads, preferred_element_type=jnp.float32
    )
    score_grad = (
        normed * (prob_grad - deltas[..., None]) * (1.0 - (capped / SOFT_CAP) ** 2)
    ).astype(jnp.bfloat16)
    return (normed.astype(jnp.bfloat16), score_grad)


def chunk_mask(query_start, key_start, tokens):
    query_pos = query_start + lax.iota(jnp.int32, tokens)
    key_pos = key_start + lax.iota(jnp.int32, tokens)
    distance = query_pos[:, None] - key_pos[None, :]
    return (key_pos[None, :] >= 0) & (distance >= 0) & (distance < WINDOW)


def picked(condition, block):
    return jnp.where(condition, block.astype(jnp.float32), 0.0)


def on_device(
    query_rows, key_rows, value_rows, out_grad, gate_grads, first_moment, second_moment, master_rows
):
    tokens = query_rows.shape[1]
    group_size = HEADS // KV_HEADS
    ctx_index = lax.axis_index("ctx")
    reach = (WINDOW - 1) // tokens + 1
    query_heads = query_rows[0].reshape(tokens, KV_HEADS, group_size, HEAD_DIM)
    grad_heads = out_grad[0].reshape(tokens, KV_HEADS, group_size, HEAD_DIM)
    key_heads = key_rows[0].reshape(tokens, KV_HEADS, HEAD_DIM)
    value_heads = value_rows[0].reshape(tokens, KV_HEADS, HEAD_DIM)
    assert reach == RING and lax.axis_size("ctx") % RING == 0
    packed = jnp.concatenate([key_heads, value_heads], axis=2)
    half = tokens // 2
    prev = passed_along(packed, "ctx", RING)
    chunk_packed = {0: packed, RING: prev}
    ring_pos = ctx_index % RING
    everyone = set(range(RING))
    up_payload = jnp.concatenate(
        [jnp.where(ring_pos < 3, packed, prev), jnp.where(ring_pos < 2, packed[:half], prev[:half])],
        axis=0,
    )
    down_payload = jnp.concatenate(
        [jnp.where(ring_pos == 0, packed, prev), jnp.where(ring_pos < 2, packed[half:], prev[half:])],
        axis=0,
    )
    going_up = ring_send(up_payload, 1, everyone)
    going_down = ring_send(down_payload, -1, everyone)
    chunk_packed[1] = going_up[:tokens]
    chunk_packed[3] = going_down[:tokens]
    chunk_packed[2] = jnp.concatenate(
        [ring_send(going_up[tokens:], 1, everyone), ring_send(going_down[tokens:], -1, everyone)],
        axis=0,
    )
    chunk_keys = {}
    chunk_values = {}
    for c, block in chunk_packed.items():
        chunk_keys[c] = block[:, :, :HEAD_DIM]
        chunk_values[c] = block[:, :, HEAD_DIM:]
    query_start = ctx_index * tokens
    capped = {}
    weights = {}
    totals = None
    weighted = None
    for c in range(reach + 1):
        visible = chunk_mask(query_start, (ctx_index - c) * tokens, tokens)
        capped[c], weights[c] = capped_weights(query_heads, chunk_keys[c], visible)
        part_total = jnp.sum(weights[c].astype(jnp.float32), axis=3)
        part_weighted = jnp.einsum(
            "grab,bgd->agrd", weights[c], chunk_values[c], preferred_element_type=jnp.float32
        )
        totals = part_total if totals is None else totals + part_total
        weighted = part_weighted if weighted is None else weighted + part_weighted
    attended = (weighted / jnp.transpose(totals, (2, 0, 1))[..., None]).astype(jnp.bfloat16)
    deltas = jnp.transpose(
        jnp.sum(grad_heads.astype(jnp.float32) * attended.astype(jnp.float32), axis=3), (1, 2, 0)
    )
    partial_value = gate_grads[0].astype(jnp.float32)
    summed = lax.psum_scatter(
        partial_value.astype(jnp.bfloat16), "dp", scatter_dimension=1, tiled=True
    ).astype(jnp.float32)
    new_first = BETA_ONE * first_moment + (1.0 - BETA_ONE) * summed
    new_second = BETA_TWO * second_moment + (1.0 - BETA_TWO) * summed * summed
    fix_one = 1.0 - BETA_ONE**ADAM_STEP
    fix_two = 1.0 - BETA_TWO**ADAM_STEP
    new_master = master_rows - LEARN_RATE * (new_first / fix_one) / (
        jnp.sqrt(new_second / fix_two) + EPSILON
    )
    gate_bf16, deltas = lax.optimization_barrier((new_master.astype(jnp.bfloat16), deltas))
    query_acc = None
    parts = {}
    for c in (3, 2, 1, RING, 0):
        if c == 0:
            returned_1 = going_down[:tokens]
            returned_2 = jnp.concatenate([relay_a, relay_b], axis=0)
            returned_3 = going_up[:tokens]
            prev_in = (
                picked(ring_pos != 0, returned_3)
                + picked(ring_pos == RING - 1, returned_1)
                + picked(ring_pos >= 2, returned_2)
            )
            own_in = (
                picked(ring_pos == 0, returned_3)
                + picked(ring_pos <= RING - 2, returned_1)
                + picked(ring_pos <= 1, returned_2)
            )
            prev_out, capped[0], weights[0] = lax.optimization_barrier(
                ((parts[RING] + prev_in).astype(jnp.bfloat16), capped[0], weights[0])
            )
        rounded, score_grad = score_terms(
            grad_heads, chunk_values[c], capped[c], weights[c], totals, deltas
        )
        part_query = jnp.einsum(
            "grab,bgd->agrd", score_grad, chunk_keys[c], preferred_element_type=jnp.float32
        )
        query_acc = part_query if query_acc is None else query_acc + part_query
        key_part = jnp.einsum(
            "grab,agrd->bgd", score_grad, query_heads, preferred_element_type=jnp.float32
        )
        value_part = jnp.einsum(
            "grab,agrd->bgd", rounded, grad_heads, preferred_element_type=jnp.float32
        )
        parts[c] = jnp.concatenate([key_part, value_part], axis=2)
        if c == 2:
            out3 = parts[3].astype(jnp.bfloat16)
            out2 = parts[2].astype(jnp.bfloat16)
            going_up = ring_send(jnp.concatenate([out3, out2[half:]], axis=0), 1, everyone)
        elif c == 1:
            out1 = parts[1].astype(jnp.bfloat16)
            going_down = ring_send(jnp.concatenate([out1, out2[:half]], axis=0), -1, everyone)
            relay_b = ring_send(going_up[tokens:], 1, everyone)
            relay_a = ring_send(going_down[tokens:], -1, everyone)
    own_acc = parts[0] + own_in
    own_acc = own_acc + passed_along(prev_out, "ctx", -RING).astype(jnp.float32)
    key_acc = own_acc[:, :, :HEAD_DIM]
    value_acc = own_acc[:, :, HEAD_DIM:]
    query_grad = (query_acc * SCORE_SCALE).astype(jnp.bfloat16)
    query_out = query_grad.reshape(1, tokens, HEADS * HEAD_DIM)
    key_out = (key_acc * SCORE_SCALE).astype(jnp.bfloat16).reshape(1, tokens, KV_HEADS * HEAD_DIM)
    value_out = value_acc.astype(jnp.bfloat16).reshape(1, tokens, KV_HEADS * HEAD_DIM)
    gate_params = lax.all_gather(gate_bf16, "dp", axis=1, tiled=True)
    return (query_out, key_out, value_out, gate_params, new_first, new_second, new_master)


def solution(mesh):
    placed = (
        P("dp", "ctx", None),
        P("dp", "ctx", None),
        P("dp", "ctx", None),
        P("dp", "ctx", None),
        P("dp", "ctx", None),
        P("ctx", "dp"),
        P("ctx", "dp"),
        P("ctx", "dp"),
    )
    return jax.shard_map(
        on_device,
        mesh=mesh,
        in_specs=placed,
        out_specs=(
            P("dp", "ctx", None),
            P("dp", "ctx", None),
            P("dp", "ctx", None),
            P("ctx", None),
            P("ctx", "dp"),
            P("ctx", "dp"),
            P("ctx", "dp"),
        ),
        check_vma=False,
    )
```

```python
import jax
import jax.numpy as jnp
from jax import lax
from jax.sharding import PartitionSpec as P

HEADS = 16
KV_HEADS = 8
HEAD_DIM = 128
WINDOW = 1024
ADAM_STEP = 10


SOFT_CAP = 50.0
SCORE_SCALE = 1.0 / 12.0
LEARN_RATE = 0.01
BETA_ONE = 0.9
BETA_TWO = 0.95
EPSILON = 1e-08


def passed_along(block, axis, distance):
    devices = range(lax.axis_size(axis))
    route = [(i - distance, i) for i in devices if i - distance in devices]
    return lax.ppermute(block, axis, route)


RING = 4


def ring_send(block, delta, senders):
    count = lax.axis_size("ctx")
    route = []
    for c in range(count):
        y = c % RING
        if y in senders:
            route.append((c, c - y + (y + delta) % RING))
    return lax.ppermute(block, "ctx", route)


def window_mask(query_start, key_start, query_count, key_count, seq_len):
    query_pos = query_start + lax.iota(jnp.int32, query_count)
    key_pos = key_start + lax.iota(jnp.int32, key_count)
    distance = query_pos[:, None] - key_pos[None, :]
    visible = (
        (key_pos[None, :] >= 0)
        & (query_pos[:, None] < seq_len)
        & (distance >= 0)
        & (distance < WINDOW)
    )
    return (visible, query_pos < seq_len)


def capped_weights(query_heads, key_heads, visible):
    raw_scores = (
        jnp.einsum("agrd,bgd->grab", query_heads, key_heads, preferred_element_type=jnp.float32)
        * SCORE_SCALE
    )
    capped = SOFT_CAP * jnp.tanh(raw_scores / SOFT_CAP)
    weights = jnp.where(visible[None, None], jnp.exp(capped), 0.0).astype(jnp.bfloat16)
    return (capped, weights)


def score_terms(grad_heads, value_heads, capped, weights, totals, deltas):
    normed = weights.astype(jnp.float32) / totals[..., None]
    prob_grad = jnp.einsum(
        "agrd,bgd->grab", grad_heads, value_heads, preferred_element_type=jnp.float32
    )
    score_grad = (
        normed * (prob_grad - deltas[..., None]) * (1.0 - (capped / SOFT_CAP) ** 2)
    ).astype(jnp.bfloat16)
    return (normed.astype(jnp.bfloat16), score_grad)


def chunk_mask(query_start, key_start, tokens):
    query_pos = query_start + lax.iota(jnp.int32, tokens)
    key_pos = key_start + lax.iota(jnp.int32, tokens)
    distance = query_pos[:, None] - key_pos[None, :]
    return (key_pos[None, :] >= 0) & (distance >= 0) & (distance < WINDOW)


def picked(condition, block):
    return jnp.where(condition, block.astype(jnp.float32), 0.0)


def on_device(
    query_rows, key_rows, value_rows, out_grad, gate_grads, first_moment, second_moment, master_rows
):
    tokens = query_rows.shape[1]
    group_size = HEADS // KV_HEADS
    ctx_index = lax.axis_index("ctx")
    reach = (WINDOW - 1) // tokens + 1
    query_heads = query_rows[0].reshape(tokens, KV_HEADS, group_size, HEAD_DIM)
    grad_heads = out_grad[0].reshape(tokens, KV_HEADS, group_size, HEAD_DIM)
    key_heads = key_rows[0].reshape(tokens, KV_HEADS, HEAD_DIM)
    value_heads = value_rows[0].reshape(tokens, KV_HEADS, HEAD_DIM)
    assert reach == RING and lax.axis_size("ctx") % RING == 0
    packed = jnp.concatenate([key_heads, value_heads], axis=2)
    half = tokens // 2
    prev = passed_along(packed, "ctx", RING)
    gate_in, prev = lax.optimization_barrier((gate_grads[0], prev))
    chunk_packed = {0: packed, RING: prev}
    ring_pos = ctx_index % RING
    everyone = set(range(RING))
    up_payload = jnp.concatenate(
        [jnp.where(ring_pos < 3, packed, prev), jnp.where(ring_pos < 2, packed[:half], prev[:half])],
        axis=0,
    )
    down_payload = jnp.concatenate(
        [jnp.where(ring_pos == 0, packed, prev), jnp.where(ring_pos < 2, packed[half:], prev[half:])],
        axis=0,
    )
    going_up = ring_send(up_payload, 1, everyone)
    going_down = ring_send(down_payload, -1, everyone)
    chunk_packed[1] = going_up[:tokens]
    chunk_packed[3] = going_down[:tokens]
    chunk_packed[2] = jnp.concatenate(
        [ring_send(going_up[tokens:], 1, everyone), ring_send(going_down[tokens:], -1, everyone)],
        axis=0,
    )
    chunk_keys = {}
    chunk_values = {}
    for c, block in chunk_packed.items():
        chunk_keys[c] = block[:, :, :HEAD_DIM]
        chunk_values[c] = block[:, :, HEAD_DIM:]
    query_start = ctx_index * tokens
    capped = {}
    weights = {}
    totals = None
    weighted = None
    for c in range(reach + 1):
        visible = chunk_mask(query_start, (ctx_index - c) * tokens, tokens)
        capped[c], weights[c] = capped_weights(query_heads, chunk_keys[c], visible)
        part_total = jnp.sum(weights[c].astype(jnp.float32), axis=3)
        part_weighted = jnp.einsum(
            "grab,bgd->agrd", weights[c], chunk_values[c], preferred_element_type=jnp.float32
        )
        totals = part_total if totals is None else totals + part_total
        weighted = part_weighted if weighted is None else weighted + part_weighted
    attended = (weighted / jnp.transpose(totals, (2, 0, 1))[..., None]).astype(jnp.bfloat16)
    deltas = jnp.transpose(
        jnp.sum(grad_heads.astype(jnp.float32) * attended.astype(jnp.float32), axis=3), (1, 2, 0)
    )
    partial_value = gate_in.astype(jnp.float32)
    summed = lax.psum_scatter(
        partial_value.astype(jnp.bfloat16), "dp", scatter_dimension=1, tiled=True
    ).astype(jnp.float32)
    new_first = BETA_ONE * first_moment + (1.0 - BETA_ONE) * summed
    new_second = BETA_TWO * second_moment + (1.0 - BETA_TWO) * summed * summed
    fix_one = 1.0 - BETA_ONE**ADAM_STEP
    fix_two = 1.0 - BETA_TWO**ADAM_STEP
    new_master = master_rows - LEARN_RATE * (new_first / fix_one) / (
        jnp.sqrt(new_second / fix_two) + EPSILON
    )
    gate_bf16, deltas = lax.optimization_barrier((new_master.astype(jnp.bfloat16), deltas))
    query_acc = None
    parts = {}
    for c in (3, 2, 1, RING, 0):
        if c == 0:
            returned_1 = going_down[:tokens]
            returned_2 = jnp.concatenate([relay_a, relay_b], axis=0)
            returned_3 = going_up[:tokens]
            prev_in = (
                picked(ring_pos != 0, returned_3)
                + picked(ring_pos == RING - 1, returned_1)
                + picked(ring_pos >= 2, returned_2)
            )
            own_in = (
                picked(ring_pos == 0, returned_3)
                + picked(ring_pos <= RING - 2, returned_1)
                + picked(ring_pos <= 1, returned_2)
            )
            prev_out, capped[0], weights[0] = lax.optimization_barrier(
                ((parts[RING] + prev_in).astype(jnp.bfloat16), capped[0], weights[0])
            )
        rounded, score_grad = score_terms(
            grad_heads, chunk_values[c], capped[c], weights[c], totals, deltas
        )
        part_query = jnp.einsum(
            "grab,bgd->agrd", score_grad, chunk_keys[c], preferred_element_type=jnp.float32
        )
        query_acc = part_query if query_acc is None else query_acc + part_query
        key_part = jnp.einsum(
            "grab,agrd->bgd", score_grad, query_heads, preferred_element_type=jnp.float32
        )
        value_part = jnp.einsum(
            "grab,agrd->bgd", rounded, grad_heads, preferred_element_type=jnp.float32
        )
        parts[c] = jnp.concatenate([key_part, value_part], axis=2)
        if c == 2:
            out3 = parts[3].astype(jnp.bfloat16)
            out2 = parts[2].astype(jnp.bfloat16)
            going_up = ring_send(jnp.concatenate([out3, out2[half:]], axis=0), 1, everyone)
        elif c == 1:
            out1 = parts[1].astype(jnp.bfloat16)
            going_down = ring_send(jnp.concatenate([out1, out2[:half]], axis=0), -1, everyone)
            relay_b = ring_send(going_up[tokens:], 1, everyone)
            relay_a = ring_send(going_down[tokens:], -1, everyone)
    own_acc = parts[0] + own_in
    own_acc = own_acc + passed_along(prev_out, "ctx", -RING).astype(jnp.float32)
    key_acc = own_acc[:, :, :HEAD_DIM]
    value_acc = own_acc[:, :, HEAD_DIM:]
    query_grad = (query_acc * SCORE_SCALE).astype(jnp.bfloat16)
    query_out = query_grad.reshape(1, tokens, HEADS * HEAD_DIM)
    key_out = (key_acc * SCORE_SCALE).astype(jnp.bfloat16).reshape(1, tokens, KV_HEADS * HEAD_DIM)
    value_out = value_acc.astype(jnp.bfloat16).reshape(1, tokens, KV_HEADS * HEAD_DIM)
    gate_params = lax.all_gather(gate_bf16, "dp", axis=1, tiled=True)
    return (query_out, key_out, value_out, gate_params, new_first, new_second, new_master)


def solution(mesh):
    placed = (
        P("dp", "ctx", None),
        P("dp", "ctx", None),
        P("dp", "ctx", None),
        P("dp", "ctx", None),
        P("dp", "ctx", None),
        P("ctx", "dp"),
        P("ctx", "dp"),
        P("ctx", "dp"),
    )
    return jax.shard_map(
        on_device,
        mesh=mesh,
        in_specs=placed,
        out_specs=(
            P("dp", "ctx", None),
            P("dp", "ctx", None),
            P("dp", "ctx", None),
            P("ctx", None),
            P("ctx", "dp"),
            P("ctx", "dp"),
            P("ctx", "dp"),
        ),
        check_vma=False,
    )
```

```python
import jax
import jax.numpy as jnp
from jax import lax
from jax.sharding import PartitionSpec as P

HEADS = 16
KV_HEADS = 8
HEAD_DIM = 128
WINDOW = 1024
ADAM_STEP = 10


SOFT_CAP = 50.0
SCORE_SCALE = 1.0 / 12.0
LEARN_RATE = 0.01
BETA_ONE = 0.9
BETA_TWO = 0.95
EPSILON = 1e-08


def passed_along(block, axis, distance):
    devices = range(lax.axis_size(axis))
    route = [(i - distance, i) for i in devices if i - distance in devices]
    return lax.ppermute(block, axis, route)


RING = 4


def ring_send(block, delta, senders):
    count = lax.axis_size("ctx")
    route = []
    for c in range(count):
        y = c % RING
        if y in senders:
            route.append((c, c - y + (y + delta) % RING))
    return lax.ppermute(block, "ctx", route)


def window_mask(query_start, key_start, query_count, key_count, seq_len):
    query_pos = query_start + lax.iota(jnp.int32, query_count)
    key_pos = key_start + lax.iota(jnp.int32, key_count)
    distance = query_pos[:, None] - key_pos[None, :]
    visible = (
        (key_pos[None, :] >= 0)
        & (query_pos[:, None] < seq_len)
        & (distance >= 0)
        & (distance < WINDOW)
    )
    return (visible, query_pos < seq_len)


def capped_weights(query_heads, key_heads, visible):
    raw_scores = (
        jnp.einsum("agrd,bgd->grab", query_heads, key_heads, preferred_element_type=jnp.float32)
        * SCORE_SCALE
    )
    capped = SOFT_CAP * jnp.tanh(raw_scores / SOFT_CAP)
    weights = jnp.where(visible[None, None], jnp.exp(capped), 0.0).astype(jnp.bfloat16)
    return (capped, weights)


def score_terms(grad_heads, value_heads, capped, weights, totals, deltas):
    normed = weights.astype(jnp.float32) / totals[..., None]
    prob_grad = jnp.einsum(
        "agrd,bgd->grab", grad_heads, value_heads, preferred_element_type=jnp.float32
    )
    score_grad = (
        normed * (prob_grad - deltas[..., None]) * (1.0 - (capped / SOFT_CAP) ** 2)
    ).astype(jnp.bfloat16)
    return (normed.astype(jnp.bfloat16), score_grad)


def chunk_mask(query_start, key_start, tokens):
    query_pos = query_start + lax.iota(jnp.int32, tokens)
    key_pos = key_start + lax.iota(jnp.int32, tokens)
    distance = query_pos[:, None] - key_pos[None, :]
    return (key_pos[None, :] >= 0) & (distance >= 0) & (distance < WINDOW)


def picked(condition, block):
    return jnp.where(condition, block.astype(jnp.float32), 0.0)


def on_device(
    query_rows, key_rows, value_rows, out_grad, gate_grads, first_moment, second_moment, master_rows
):
    tokens = query_rows.shape[1]
    group_size = HEADS // KV_HEADS
    ctx_index = lax.axis_index("ctx")
    reach = (WINDOW - 1) // tokens + 1
    query_heads = query_rows[0].reshape(tokens, KV_HEADS, group_size, HEAD_DIM)
    grad_heads = out_grad[0].reshape(tokens, KV_HEADS, group_size, HEAD_DIM)
    key_heads = key_rows[0].reshape(tokens, KV_HEADS, HEAD_DIM)
    value_heads = value_rows[0].reshape(tokens, KV_HEADS, HEAD_DIM)
    assert reach == RING and lax.axis_size("ctx") % RING == 0
    packed = jnp.concatenate([key_heads, value_heads], axis=2)
    half = tokens // 2
    prev = passed_along(packed, "ctx", RING)
    chunk_packed = {0: packed, RING: prev}
    ring_pos = ctx_index % RING
    everyone = set(range(RING))
    up_payload = jnp.concatenate(
        [jnp.where(ring_pos < 3, packed, prev), jnp.where(ring_pos < 2, packed[:half], prev[:half])],
        axis=0,
    )
    down_payload = jnp.concatenate(
        [jnp.where(ring_pos == 0, packed, prev), jnp.where(ring_pos < 2, packed[half:], prev[half:])],
        axis=0,
    )
    going_up = ring_send(up_payload, 1, everyone)
    going_down = ring_send(down_payload, -1, everyone)
    chunk_packed[1] = going_up[:tokens]
    chunk_packed[3] = going_down[:tokens]
    chunk_packed[2] = jnp.concatenate(
        [ring_send(going_up[tokens:], 1, everyone), ring_send(going_down[tokens:], -1, everyone)],
        axis=0,
    )
    chunk_keys = {}
    chunk_values = {}
    for c, block in chunk_packed.items():
        chunk_keys[c] = block[:, :, :HEAD_DIM]
        chunk_values[c] = block[:, :, HEAD_DIM:]
    query_start = ctx_index * tokens
    capped = {}
    weights = {}
    totals = None
    weighted = None
    for c in range(reach + 1):
        visible = chunk_mask(query_start, (ctx_index - c) * tokens, tokens)
        capped[c], weights[c] = capped_weights(query_heads, chunk_keys[c], visible)
        part_total = jnp.sum(weights[c].astype(jnp.float32), axis=3)
        part_weighted = jnp.einsum(
            "grab,bgd->agrd", weights[c], chunk_values[c], preferred_element_type=jnp.float32
        )
        totals = part_total if totals is None else totals + part_total
        weighted = part_weighted if weighted is None else weighted + part_weighted
    attended = (weighted / jnp.transpose(totals, (2, 0, 1))[..., None]).astype(jnp.bfloat16)
    deltas = jnp.transpose(
        jnp.sum(grad_heads.astype(jnp.float32) * attended.astype(jnp.float32), axis=3), (1, 2, 0)
    )
    partial_value = gate_grads[0].astype(jnp.float32)
    summed = lax.psum_scatter(
        partial_value.astype(jnp.bfloat16), "dp", scatter_dimension=1, tiled=True
    ).astype(jnp.float32)
    new_first = BETA_ONE * first_moment + (1.0 - BETA_ONE) * summed
    new_second = BETA_TWO * second_moment + (1.0 - BETA_TWO) * summed * summed
    fix_one = 1.0 - BETA_ONE**ADAM_STEP
    fix_two = 1.0 - BETA_TWO**ADAM_STEP
    new_master = master_rows - LEARN_RATE * (new_first / fix_one) / (
        jnp.sqrt(new_second / fix_two) + EPSILON
    )
    gate_bf16, deltas = lax.optimization_barrier((new_master.astype(jnp.bfloat16), deltas))
    query_acc = None
    parts = {}
    for c in (3, 1, 2, RING, 0):
        if c == 0:
            returned_1 = back_1
            returned_2 = jnp.concatenate([relay_a, relay_b], axis=0)
            returned_3 = back_3
            prev_in = (
                picked(ring_pos != 0, returned_3)
                + picked(ring_pos == RING - 1, returned_1)
                + picked(ring_pos >= 2, returned_2)
            )
            own_in = (
                picked(ring_pos == 0, returned_3)
                + picked(ring_pos <= RING - 2, returned_1)
                + picked(ring_pos <= 1, returned_2)
            )
            prev_out, capped[0], weights[0] = lax.optimization_barrier(
                ((parts[RING] + prev_in).astype(jnp.bfloat16), capped[0], weights[0])
            )
        rounded, score_grad = score_terms(
            grad_heads, chunk_values[c], capped[c], weights[c], totals, deltas
        )
        part_query = jnp.einsum(
            "grab,bgd->agrd", score_grad, chunk_keys[c], preferred_element_type=jnp.float32
        )
        query_acc = part_query if query_acc is None else query_acc + part_query
        key_part = jnp.einsum(
            "grab,agrd->bgd", score_grad, query_heads, preferred_element_type=jnp.float32
        )
        value_part = jnp.einsum(
            "grab,agrd->bgd", rounded, grad_heads, preferred_element_type=jnp.float32
        )
        parts[c] = jnp.concatenate([key_part, value_part], axis=2)
        if c == 3:
            back_3 = ring_send(parts[3].astype(jnp.bfloat16), 1, everyone)
        elif c == 1:
            back_1 = ring_send(parts[1].astype(jnp.bfloat16), -1, everyone)
        elif c == 2:
            out2 = parts[2].astype(jnp.bfloat16)
            relay_b = ring_send(ring_send(out2[half:], 1, everyone), 1, everyone)
            relay_a = ring_send(ring_send(out2[:half], -1, everyone), -1, everyone)
    own_acc = parts[0] + own_in
    own_acc = own_acc + passed_along(prev_out, "ctx", -RING).astype(jnp.float32)
    key_acc = own_acc[:, :, :HEAD_DIM]
    value_acc = own_acc[:, :, HEAD_DIM:]
    query_grad = (query_acc * SCORE_SCALE).astype(jnp.bfloat16)
    query_out = query_grad.reshape(1, tokens, HEADS * HEAD_DIM)
    key_out = (key_acc * SCORE_SCALE).astype(jnp.bfloat16).reshape(1, tokens, KV_HEADS * HEAD_DIM)
    value_out = value_acc.astype(jnp.bfloat16).reshape(1, tokens, KV_HEADS * HEAD_DIM)
    gate_params = lax.all_gather(gate_bf16, "dp", axis=1, tiled=True)
    return (query_out, key_out, value_out, gate_params, new_first, new_second, new_master)


def solution(mesh):
    placed = (
        P("dp", "ctx", None),
        P("dp", "ctx", None),
        P("dp", "ctx", None),
        P("dp", "ctx", None),
        P("dp", "ctx", None),
        P("ctx", "dp"),
        P("ctx", "dp"),
        P("ctx", "dp"),
    )
    return jax.shard_map(
        on_device,
        mesh=mesh,
        in_specs=placed,
        out_specs=(
            P("dp", "ctx", None),
            P("dp", "ctx", None),
            P("dp", "ctx", None),
            P("ctx", None),
            P("ctx", "dp"),
            P("ctx", "dp"),
            P("ctx", "dp"),
        ),
        check_vma=False,
    )
```

```python
import jax
import jax.numpy as jnp
from jax import lax
from jax.sharding import PartitionSpec as P

HEADS = 16
KV_HEADS = 8
HEAD_DIM = 128
WINDOW = 1024
ADAM_STEP = 10


SOFT_CAP = 50.0
SCORE_SCALE = 1.0 / 12.0
LEARN_RATE = 0.01
BETA_ONE = 0.9
BETA_TWO = 0.95
EPSILON = 1e-08


def passed_along(block, axis, distance):
    devices = range(lax.axis_size(axis))
    route = [(i - distance, i) for i in devices if i - distance in devices]
    return lax.ppermute(block, axis, route)


RING = 4


def ring_send(block, delta, senders):
    count = lax.axis_size("ctx")
    route = []
    for c in range(count):
        y = c % RING
        if y in senders:
            route.append((c, c - y + (y + delta) % RING))
    return lax.ppermute(block, "ctx", route)


def window_mask(query_start, key_start, query_count, key_count, seq_len):
    query_pos = query_start + lax.iota(jnp.int32, query_count)
    key_pos = key_start + lax.iota(jnp.int32, key_count)
    distance = query_pos[:, None] - key_pos[None, :]
    visible = (
        (key_pos[None, :] >= 0)
        & (query_pos[:, None] < seq_len)
        & (distance >= 0)
        & (distance < WINDOW)
    )
    return (visible, query_pos < seq_len)


def capped_weights(query_heads, key_heads, visible):
    raw_scores = (
        jnp.einsum("agrd,bgd->grab", query_heads, key_heads, preferred_element_type=jnp.float32)
        * SCORE_SCALE
    )
    capped = SOFT_CAP * jnp.tanh(raw_scores / SOFT_CAP)
    weights = jnp.where(visible[None, None], jnp.exp(capped), 0.0).astype(jnp.bfloat16)
    return (capped, weights)


def score_terms(grad_heads, value_heads, capped, weights, totals, deltas):
    normed = weights.astype(jnp.float32) / totals[..., None]
    prob_grad = jnp.einsum(
        "agrd,bgd->grab", grad_heads, value_heads, preferred_element_type=jnp.float32
    )
    score_grad = (
        normed * (prob_grad - deltas[..., None]) * (1.0 - (capped / SOFT_CAP) ** 2)
    ).astype(jnp.bfloat16)
    return (normed.astype(jnp.bfloat16), score_grad)


def chunk_mask(query_start, key_start, tokens):
    query_pos = query_start + lax.iota(jnp.int32, tokens)
    key_pos = key_start + lax.iota(jnp.int32, tokens)
    distance = query_pos[:, None] - key_pos[None, :]
    return (key_pos[None, :] >= 0) & (distance >= 0) & (distance < WINDOW)


def picked(condition, block):
    return jnp.where(condition, block.astype(jnp.float32), 0.0)


def on_device(
    query_rows, key_rows, value_rows, out_grad, gate_grads, first_moment, second_moment, master_rows
):
    tokens = query_rows.shape[1]
    group_size = HEADS // KV_HEADS
    ctx_index = lax.axis_index("ctx")
    reach = (WINDOW - 1) // tokens + 1
    query_heads = query_rows[0].reshape(tokens, KV_HEADS, group_size, HEAD_DIM)
    grad_heads = out_grad[0].reshape(tokens, KV_HEADS, group_size, HEAD_DIM)
    key_heads = key_rows[0].reshape(tokens, KV_HEADS, HEAD_DIM)
    value_heads = value_rows[0].reshape(tokens, KV_HEADS, HEAD_DIM)
    assert reach == RING and lax.axis_size("ctx") % RING == 0
    packed = jnp.concatenate([key_heads, value_heads], axis=2)
    half = tokens // 2
    prev = passed_along(packed, "ctx", RING)
    chunk_packed = {0: packed, RING: prev}
    ring_pos = ctx_index % RING
    everyone = set(range(RING))
    up_payload = jnp.concatenate(
        [jnp.where(ring_pos < 3, packed, prev), jnp.where(ring_pos < 2, packed[:half], prev[:half])],
        axis=0,
    )
    down_payload = jnp.concatenate(
        [jnp.where(ring_pos == 0, packed, prev), jnp.where(ring_pos < 2, packed[half:], prev[half:])],
        axis=0,
    )
    going_up = ring_send(up_payload, 1, everyone)
    going_down = ring_send(down_payload, -1, everyone)
    chunk_packed[1] = going_up[:tokens]
    chunk_packed[3] = going_down[:tokens]
    chunk_packed[2] = jnp.concatenate(
        [ring_send(going_up[tokens:], 1, everyone), ring_send(going_down[tokens:], -1, everyone)],
        axis=0,
    )
    chunk_keys = {}
    chunk_values = {}
    for c, block in chunk_packed.items():
        chunk_keys[c] = block[:, :, :HEAD_DIM]
        chunk_values[c] = block[:, :, HEAD_DIM:]
    query_start = ctx_index * tokens
    capped = {}
    weights = {}
    totals = None
    weighted = None
    for c in range(reach + 1):
        visible = chunk_mask(query_start, (ctx_index - c) * tokens, tokens)
        capped[c], weights[c] = capped_weights(query_heads, chunk_keys[c], visible)
        part_total = jnp.sum(weights[c].astype(jnp.float32), axis=3)
        part_weighted = jnp.einsum(
            "grab,bgd->agrd", weights[c], chunk_values[c], preferred_element_type=jnp.float32
        )
        totals = part_total if totals is None else totals + part_total
        weighted = part_weighted if weighted is None else weighted + part_weighted
    attended = (weighted / jnp.transpose(totals, (2, 0, 1))[..., None]).astype(jnp.bfloat16)
    deltas = jnp.transpose(
        jnp.sum(grad_heads.astype(jnp.float32) * attended.astype(jnp.float32), axis=3), (1, 2, 0)
    )
    partial_value = gate_grads[0].astype(jnp.float32)
    summed = lax.psum_scatter(
        partial_value.astype(jnp.bfloat16), "dp", scatter_dimension=1, tiled=True
    ).astype(jnp.float32)
    new_first = BETA_ONE * first_moment + (1.0 - BETA_ONE) * summed
    new_second = BETA_TWO * second_moment + (1.0 - BETA_TWO) * summed * summed
    fix_one = 1.0 - BETA_ONE**ADAM_STEP
    fix_two = 1.0 - BETA_TWO**ADAM_STEP
    new_master = master_rows - LEARN_RATE * (new_first / fix_one) / (
        jnp.sqrt(new_second / fix_two) + EPSILON
    )
    gate_bf16, deltas = lax.optimization_barrier((new_master.astype(jnp.bfloat16), deltas))
    query_acc = None
    parts = {}
    for c in (3, 1, 2, RING, 0):
        if c == 0:
            returned_1 = back_1
            returned_2 = jnp.concatenate([relay_a, relay_b], axis=0)
            returned_3 = back_3
            prev_in = (
                picked(ring_pos != 0, returned_3)
                + picked(ring_pos == RING - 1, returned_1)
                + picked(ring_pos >= 2, returned_2)
            )
            own_in = (
                picked(ring_pos == 0, returned_3)
                + picked(ring_pos <= RING - 2, returned_1)
                + picked(ring_pos <= 1, returned_2)
            )
        rounded, score_grad = score_terms(
            grad_heads, chunk_values[c], capped[c], weights[c], totals, deltas
        )
        part_query = jnp.einsum(
            "grab,bgd->agrd", score_grad, chunk_keys[c], preferred_element_type=jnp.float32
        )
        query_acc = part_query if query_acc is None else query_acc + part_query
        if c == 0:
            prev_out, rounded, score_grad = lax.optimization_barrier(
                ((parts[RING] + prev_in).astype(jnp.bfloat16), rounded, score_grad)
            )
        key_part = jnp.einsum(
            "grab,agrd->bgd", score_grad, query_heads, preferred_element_type=jnp.float32
        )
        value_part = jnp.einsum(
            "grab,agrd->bgd", rounded, grad_heads, preferred_element_type=jnp.float32
        )
        parts[c] = jnp.concatenate([key_part, value_part], axis=2)
        if c == 3:
            back_3 = ring_send(parts[3].astype(jnp.bfloat16), 1, everyone)
        elif c == 1:
            back_1 = ring_send(parts[1].astype(jnp.bfloat16), -1, everyone)
        elif c == 2:
            out2 = parts[2].astype(jnp.bfloat16)
            relay_b = ring_send(ring_send(out2[half:], 1, everyone), 1, everyone)
            relay_a = ring_send(ring_send(out2[:half], -1, everyone), -1, everyone)
    own_acc = parts[0] + own_in
    own_acc = own_acc + passed_along(prev_out, "ctx", -RING).astype(jnp.float32)
    key_acc = own_acc[:, :, :HEAD_DIM]
    value_acc = own_acc[:, :, HEAD_DIM:]
    query_grad = (query_acc * SCORE_SCALE).astype(jnp.bfloat16)
    query_out = query_grad.reshape(1, tokens, HEADS * HEAD_DIM)
    key_out = (key_acc * SCORE_SCALE).astype(jnp.bfloat16).reshape(1, tokens, KV_HEADS * HEAD_DIM)
    value_out = value_acc.astype(jnp.bfloat16).reshape(1, tokens, KV_HEADS * HEAD_DIM)
    gate_params = lax.all_gather(gate_bf16, "dp", axis=1, tiled=True)
    return (query_out, key_out, value_out, gate_params, new_first, new_second, new_master)


def solution(mesh):
    placed = (
        P("dp", "ctx", None),
        P("dp", "ctx", None),
        P("dp", "ctx", None),
        P("dp", "ctx", None),
        P("dp", "ctx", None),
        P("ctx", "dp"),
        P("ctx", "dp"),
        P("ctx", "dp"),
    )
    return jax.shard_map(
        on_device,
        mesh=mesh,
        in_specs=placed,
        out_specs=(
            P("dp", "ctx", None),
            P("dp", "ctx", None),
            P("dp", "ctx", None),
            P("ctx", None),
            P("ctx", "dp"),
            P("ctx", "dp"),
            P("ctx", "dp"),
        ),
        check_vma=False,
    )
```
